128 devices in a mesh: tm: 8 (over y_hi, x), space: 16 (over y_lo, z, core).
Axes of the slice: x: 4, y: 4 (y_hi: 2, y_lo: 2; y = y_hi * 2 + y_lo), z: 4, core: 2. Of those that a mesh axis runs over, the one named last changes fastest.
Arguments:
- video: bfloat16 [2, 16, 32, 48, 384], P(None, 'tm', 'space'), may hold values from -6 to 6
- conv_weight: bfloat16 [10368, 384], replicated, may hold values from -0.0625 to 0.0625
- norm_gain: bfloat16 [384], replicated, may hold values from 0.099609375 to 1.8984375
- down_weight: bfloat16 [3456, 384], replicated, may hold values from -0.109375 to 0.109375
- clip_lengths: int32 [2], replicated, may hold values from 1 to 16, as said below
- cotangent: bfloat16 [2, 16, 16, 24, 384], P(None, 'tm', 'space'), may hold values from -6 to 6
Outputs:
- latent: bfloat16 [2, 16, 16, 24, 384], P(None, 'tm', 'space')
- grad_conv: float32 [3981312], P(('tm', 'space'))
- grad_down: float32 [1327104], P(('tm', 'space'))
The draws below stay inside these ranges and needn't reach their ends.
Inputs may be any that keep to these rules, and one draw needn't show every extreme that they name: `clip_lengths`: clip 0 is full, with 16 valid frames.
All inputs are finite; a program needn't handle non-finite values.
Results may differ from the reference program's by a relative error of at most 0.015.
Values may be sent and summed in bfloat16 or wider, within the bound.
No kernel may reach another device: no remote copies, remote signals or barrier semaphores. Data moves between devices by JAX's collectives and lax.ppermute only.
A program may use at most 128 MiB of HBM per device.

```python
import jax
import jax.numpy as jnp
from jax import lax

C = 384
CLIPS = 2
W = 48
FRAMES = 16
HEIGHT = 32


def draw_clip_lengths(key, part):
    others = jax.random.randint(key, (CLIPS - 1,), 1, FRAMES + 1, dtype=jnp.int32)
    return jnp.concatenate([jnp.full((1,), FRAMES, jnp.int32), others])


def block_scale(stream_key, dims, split, low, high):
    def one(position, parts):
        draws = jax.random.uniform(jax.random.fold_in(jax.random.fold_in(stream_key, 6), position), (parts,), jnp.float32, low / len(split), high / len(split))
        return jnp.repeat(jnp.exp(draws), dims[position] // parts).reshape((-1,) + (1,) * (len(dims) - position - 1))

    gain = one(*split[0])
    for cut in split[1:]:
        gain = gain * one(*cut)
    return gain


def scatter_about(rng, shape, scale, bound, shards=(), kind=jnp.bfloat16):
    values = jax.random.normal(rng, shape, jnp.float32) * scale
    if len(shards) > 0:
        values = block_scale(rng, shape, shards, -0.22, 0.18) * values
    return jnp.clip(values, min=-bound, max=bound).astype(kind)


def setup_inputs(seed: int = 0) -> dict:
    key_of = jax.random.split(jax.random.key(seed), 7)
    video = scatter_about(key_of[0], (CLIPS, FRAMES, HEIGHT, W, C), 1.0, 6.0, ((1, 8), (2, 16)))
    conv_weight = scatter_about(key_of[1], (27 * C, C), (27 * C) ** -0.5, 0.0625)
    norm_gain = jnp.clip(1.0 + 0.18 * jax.random.normal(key_of[2], (C,), jnp.float32), 0.099609375, 1.8984375).astype(jnp.bfloat16)
    down_weight = scatter_about(key_of[3], (9 * C, C), (9 * C) ** -0.5, 0.109375)
    clip_lengths = draw_clip_lengths(jax.random.fold_in(key_of[6], 71), 0)
    cotangent = scatter_about(key_of[5], (CLIPS, FRAMES, HEIGHT // 2, W // 2, C), 1.0, 6.0, ((1, 8), (2, 16)))
    return {"video": video, "conv_weight": conv_weight, "norm_gain": norm_gain, "down_weight": down_weight, "clip_lengths": clip_lengths, "cotangent": cotangent}


EPSILON = 1e-06

def norm_act(conv_out, norm_gain, keeper):
    scale = lax.rsqrt(lax.optimization_barrier(jnp.mean(conv_out * conv_out, axis=-1, keepdims=True)) + EPSILON)
    normed = conv_out * scale * norm_gain.astype(jnp.float32)
    return (normed * jax.nn.sigmoid(normed) * keeper).astype(jnp.bfloat16)

def norm_back(conv_out, norm_gain, keeper, upstream):
    scale = lax.rsqrt(lax.optimization_barrier(jnp.mean(conv_out * conv_out, axis=-1, keepdims=True)) + EPSILON)
    unit = conv_out * scale
    gained = norm_gain.astype(jnp.float32)
    normed = unit * gained
    sigma = jax.nn.sigmoid(normed)
    d_normed = upstream * keeper * sigma * (1.0 + normed * (1.0 - sigma))
    d_unit = d_normed * gained
    return (scale * (d_unit - unit * lax.optimization_barrier(jnp.mean(d_unit * unit, axis=-1, keepdims=True)))).astype(jnp.bfloat16)

def conv_window(padded, tap, frames, rows, start):
    width = padded.shape[3] - 2
    frame_tap = tap // 9
    row_tap = tap // 3 % 3
    col_tap = tap % 3
    return padded[:, frame_tap:frame_tap + frames, start + row_tap:start + row_tap + rows, col_tap:col_tap + width]

def causal_conv(padded, conv_weight, frames, rows, start):
    channels = padded.shape[-1]
    width = padded.shape[3] - 2
    shape = (padded.shape[0], frames, rows, width, channels)
    total = jnp.zeros(shape, jnp.float32)
    for tap in range(27):
        window = conv_window(padded, tap, frames, rows, start).reshape(-1, channels)
        block = conv_weight[tap * channels:(tap + 1) * channels]
        total = total + jnp.dot(window, block, preferred_element_type=jnp.float32).reshape(shape)
    return total

def conv_weight_grad(padded, d_conv, frames, rows, start):
    channels = padded.shape[-1]
    flat_grad = d_conv.reshape(-1, channels)
    blocks = []
    for tap in range(27):
        window = conv_window(padded, tap, frames, rows, start).reshape(-1, channels)
        blocks.append(jnp.dot(window.T, flat_grad, preferred_element_type=jnp.float32))
    return jnp.stack(blocks).reshape(-1)

def down_window(hpad, tap):
    out_rows = (hpad.shape[2] - 1) // 2
    out_cols = (hpad.shape[3] - 1) // 2
    row_tap = tap // 3
    col_tap = tap % 3
    return hpad[:, :, row_tap:row_tap + 2 * out_rows:2, col_tap:col_tap + 2 * out_cols:2]

def down_forward(hpad, down_weight):
    channels = hpad.shape[-1]
    shape = (hpad.shape[0], hpad.shape[1], (hpad.shape[2] - 1) // 2, (hpad.shape[3] - 1) // 2, channels)
    total = jnp.zeros(shape, jnp.float32)
    for tap in range(9):
        window = down_window(hpad, tap).reshape(-1, channels)
        block = down_weight[tap * channels:(tap + 1) * channels]
        total = total + jnp.dot(window, block, preferred_element_type=jnp.float32).reshape(shape)
    return total

def down_weight_grad(hpad, cotangent):
    channels = hpad.shape[-1]
    flat_cot = cotangent.reshape(-1, channels)
    blocks = []
    for tap in range(9):
        window = down_window(hpad, tap).reshape(-1, channels)
        blocks.append(jnp.dot(window.T, flat_cot, preferred_element_type=jnp.float32))
    return jnp.stack(blocks).reshape(-1)

def down_back(hpad_shape, cotangent, down_weight):
    channels = cotangent.shape[-1]
    out_rows = cotangent.shape[2]
    out_cols = cotangent.shape[3]
    flat_cot = cotangent.reshape(-1, channels)
    d_pad = jnp.zeros(hpad_shape, jnp.float32)
    for tap in range(9):
        row_tap = tap // 3
        col_tap = tap % 3
        block = down_weight[tap * channels:(tap + 1) * channels]
        piece = jnp.dot(flat_cot, block.T, preferred_element_type=jnp.float32).reshape(cotangent.shape)
        d_pad = d_pad.at[:, :, row_tap:row_tap + 2 * out_rows:2, col_tap:col_tap + 2 * out_cols:2].add(piece)
    return d_pad

def reference(video, conv_weight, norm_gain, down_weight, clip_lengths, cotangent):
    frames = video.shape[1]
    rows = video.shape[2]
    width = video.shape[3]
    keeper = (jnp.arange(frames, dtype=jnp.int32)[None, :] < clip_lengths[:, None]).astype(jnp.float32)
    keeper = keeper[:, :, None, None, None]
    masked = video * keeper.astype(jnp.bfloat16)
    padded = jnp.pad(masked, ((0, 0), (2, 0), (1, 1), (1, 1), (0, 0)))
    conv_out = causal_conv(padded, conv_weight, frames, rows, 0)
    hidden = norm_act(conv_out, norm_gain, keeper)
    hpad = jnp.pad(hidden, ((0, 0), (0, 0), (0, 1), (0, 1), (0, 0)))
    latent = down_forward(hpad, down_weight).astype(jnp.bfloat16)
    grad_down = down_weight_grad(hpad, cotangent)
    d_hidden = down_back(hpad.shape, cotangent, down_weight)[:, :, :rows, :width]
    d_conv = norm_back(conv_out, norm_gain, keeper, d_hidden)
    grad_conv = conv_weight_grad(padded, d_conv, frames, rows, 0)
    return (latent, grad_conv, grad_down)
```

```python
import jax
import jax.numpy as jnp
from jax import lax
from jax.sharding import PartitionSpec as P

EPSILON = 1e-06


def shifted(array, axes, moves):
    sizes = [lax.axis_size(a) for a in axes]
    total = 1
    for n in sizes:
        total *= n
    pairs = []
    for src in range(total):
        coords, rest = [], src
        for n in reversed(sizes):
            coords.append(rest % n)
            rest //= n
        coords = coords[::-1]
        dst = [c + m for c, m in zip(coords, moves)]
        if all(0 <= d < n for d, n in zip(dst, sizes)):
            flat = 0
            for d, n in zip(dst, sizes):
                flat = flat * n + d
            pairs.append((src, flat))
    name = axes[0] if len(axes) == 1 else tuple(axes)
    return lax.ppermute(array, name, pairs)


def norm_act(conv_out, norm_gain, keeper):
    scale = lax.rsqrt(jnp.mean(conv_out * conv_out, axis=-1, keepdims=True) + EPSILON)
    normed = conv_out * scale * norm_gain.astype(jnp.float32)
    return (normed * jax.nn.sigmoid(normed) * keeper).astype(jnp.bfloat16)


def norm_back(conv_out, norm_gain, keeper, upstream):
    scale = lax.rsqrt(jnp.mean(conv_out * conv_out, axis=-1, keepdims=True) + EPSILON)
    unit = conv_out * scale
    gained = norm_gain.astype(jnp.float32)
    normed = unit * gained
    sigma = jax.nn.sigmoid(normed)
    d_normed = upstream * keeper * sigma * (1.0 + normed * (1.0 - sigma))
    d_unit = d_normed * gained
    return (scale * (d_unit - unit * jnp.mean(d_unit * unit, axis=-1, keepdims=True))).astype(
        jnp.bfloat16
    )


def local(video, conv_weight, norm_gain, down_weight, clip_lengths, cotangent):
    clips, frames, rows, width, channels = video.shape
    t = lax.axis_index("tm")
    s = lax.axis_index("space")
    last = lax.axis_size("space") - 1
    frame_ids = t * frames + jnp.arange(frames, dtype=jnp.int32)
    keeper = (frame_ids[None, :] < clip_lengths[:, None]).astype(jnp.float32)[
        :, :, None, None, None
    ]
    masked = video * keeper.astype(jnp.bfloat16)

    top = masked[:, :, rows - 1 :]
    above = shifted(top, ("space",), (1,))
    below = shifted(masked, ("space",), (-1,))
    prev = shifted(masked, ("tm",), (1,))
    prev_above = shifted(top, ("tm", "space"), (1, 1))
    prev_below = shifted(masked, ("tm", "space"), (1, -1))
    cot_above = shifted(cotangent, ("space",), (1,))

    own = jnp.concatenate([above, masked, below], axis=2)
    old = jnp.concatenate([prev_above, prev, prev_below], axis=2)
    padded = jnp.pad(
        jnp.concatenate([old, own], axis=1), ((0, 0), (0, 0), (0, 0), (1, 1), (0, 0))
    )

    kernel3 = conv_weight.reshape(3, 3, 3, channels, channels)
    conv_out = lax.conv_general_dilated(
        padded,
        kernel3,
        window_strides=(1, 1, 1),
        padding="VALID",
        dimension_numbers=("NDHWC", "DHWIO", "NDHWC"),
        preferred_element_type=jnp.float32,
    )
    hidden = norm_act(conv_out, norm_gain, keeper)
    row_ids = jnp.arange(rows + 1, dtype=jnp.int32)[None, None, :, None, None]
    hidden = jnp.where((row_ids < rows) | (s < last), hidden, jnp.zeros_like(hidden))
    hpad = jnp.pad(hidden, ((0, 0), (0, 0), (0, 0), (0, 1), (0, 0)))
    hflat = hpad.reshape(clips * frames, rows + 1, width + 1, channels)

    kernel2 = down_weight.reshape(3, 3, channels, channels)
    latent = lax.conv_general_dilated(
        hflat,
        kernel2,
        window_strides=(2, 2),
        padding="VALID",
        dimension_numbers=("NHWC", "HWIO", "NHWC"),
        preferred_element_type=jnp.float32,
    ).astype(jnp.bfloat16)
    latent = latent.reshape(cotangent.shape)

    cflat = cotangent.reshape(clips * frames, rows // 2, width // 2, channels)
    grad_down = lax.conv_general_dilated(
        hflat,
        cflat,
        window_strides=(1, 1),
        padding="VALID",
        rhs_dilation=(2, 2),
        dimension_numbers=("CHWN", "IHWO", "NHWC"),
        preferred_element_type=jnp.float32,
    )
    grad_down = jnp.transpose(grad_down, (1, 2, 0, 3)).reshape(9 * channels, channels)

    cot2 = jnp.concatenate([cot_above, cotangent], axis=2).reshape(
        clips * frames, rows // 2 + 1, width // 2, channels
    )
    d_hidden = lax.conv_general_dilated(
        cot2,
        kernel2[::-1, ::-1],
        window_strides=(1, 1),
        padding=((0, 1), (2, 1)),
        lhs_dilation=(2, 2),
        dimension_numbers=("NHWC", "HWOI", "NHWC"),
        preferred_element_type=jnp.float32,
    ).reshape(clips, frames, rows, width, channels)

    d_conv = norm_back(conv_out[:, :, :rows], norm_gain, keeper, d_hidden)
    grad_conv = lax.conv_general_dilated(
        padded[:, :, : rows + 2],
        d_conv,
        window_strides=(1, 1, 1),
        padding="VALID",
        dimension_numbers=("CDHWN", "IDHWO", "NDHWC"),
        preferred_element_type=jnp.float32,
    )
    grad_conv = jnp.transpose(grad_conv, (1, 2, 3, 0, 4)).reshape(27 * channels, channels)

    grad_conv, grad_down = lax.psum((grad_conv, grad_down), ("tm", "space"))
    devices = lax.axis_size("tm") * lax.axis_size("space")
    me = t * lax.axis_size("space") + s
    conv_rows = grad_conv.shape[0] // devices
    down_rows = grad_down.shape[0] // devices
    conv_share = lax.dynamic_slice_in_dim(grad_conv, me * conv_rows, conv_rows, axis=0)
    down_share = lax.dynamic_slice_in_dim(grad_down, me * down_rows, down_rows, axis=0)
    return (latent, conv_share.reshape(-1), down_share.reshape(-1))


def solution(mesh):
    in_specs = (
        P(None, "tm", "space", None, None),
        P(),
        P(),
        P(),
        P(),
        P(None, "tm", "space", None, None),
    )
    out_specs = (P(None, "tm", "space", None, None), P(("tm", "space")), P(("tm", "space")))
    return jax.shard_map(local, mesh=mesh, in_specs=in_specs, out_specs=out_specs, check_vma=False)
```

```python
import jax
import jax.numpy as jnp
from jax import lax
from jax.sharding import PartitionSpec as P

EPSILON = 1e-06


def shifted(array, axes, moves):
    sizes = [lax.axis_size(a) for a in axes]
    total = 1
    for n in sizes:
        total *= n
    pairs = []
    for src in range(total):
        coords, rest = [], src
        for n in reversed(sizes):
            coords.append(rest % n)
            rest //= n
        coords = coords[::-1]
        dst = [c + m for c, m in zip(coords, moves)]
        if all(0 <= d < n for d, n in zip(dst, sizes)):
            flat = 0
            for d, n in zip(dst, sizes):
                flat = flat * n + d
            pairs.append((src, flat))
    name = axes[0] if len(axes) == 1 else tuple(axes)
    return lax.ppermute(array, name, pairs)


def norm_act(conv_out, norm_gain, keeper):
    scale = lax.rsqrt(jnp.mean(conv_out * conv_out, axis=-1, keepdims=True) + EPSILON)
    normed = conv_out * scale * norm_gain.astype(jnp.float32)
    return (normed * jax.nn.sigmoid(normed) * keeper).astype(jnp.bfloat16)


def norm_back(conv_out, norm_gain, keeper, upstream):
    scale = lax.rsqrt(jnp.mean(conv_out * conv_out, axis=-1, keepdims=True) + EPSILON)
    unit = conv_out * scale
    gained = norm_gain.astype(jnp.float32)
    normed = unit * gained
    sigma = jax.nn.sigmoid(normed)
    d_normed = upstream * keeper * sigma * (1.0 + normed * (1.0 - sigma))
    d_unit = d_normed * gained
    return (scale * (d_unit - unit * jnp.mean(d_unit * unit, axis=-1, keepdims=True))).astype(
        jnp.bfloat16
    )


def local(video, conv_weight, norm_gain, down_weight, clip_lengths, cotangent):
    clips, frames, rows, width, channels = video.shape
    t = lax.axis_index("tm")
    s = lax.axis_index("space")
    last = lax.axis_size("space") - 1
    frame_ids = t * frames + jnp.arange(frames, dtype=jnp.int32)
    keeper = (frame_ids[None, :] < clip_lengths[:, None]).astype(jnp.float32)[
        :, :, None, None, None
    ]
    masked = video * keeper.astype(jnp.bfloat16)

    top = masked[:, :, rows - 1 :]
    above = shifted(top, ("space",), (1,))
    below = shifted(masked, ("space",), (-1,))
    prev = shifted(masked, ("tm",), (1,))
    prev_above = shifted(top, ("tm", "space"), (1, 1))
    prev_below = shifted(masked, ("tm", "space"), (1, -1))
    cot_above = shifted(cotangent, ("space",), (1,))

    own = jnp.concatenate([above, masked, below], axis=2)
    old = jnp.concatenate([prev_above, prev, prev_below], axis=2)
    padded = jnp.pad(
        jnp.concatenate([old, own], axis=1), ((0, 0), (0, 0), (0, 0), (1, 1), (0, 0))
    )

    kernel3 = conv_weight.reshape(3, 3, 3, channels, channels)
    conv_out = lax.conv_general_dilated(
        padded,
        kernel3,
        window_strides=(1, 1, 1),
        padding="VALID",
        dimension_numbers=("NDHWC", "DHWIO", "NDHWC"),
        preferred_element_type=jnp.float32,
    )
    hidden = norm_act(conv_out, norm_gain, keeper)
    row_ids = jnp.arange(rows + 1, dtype=jnp.int32)[None, None, :, None, None]
    hidden = jnp.where((row_ids < rows) | (s < last), hidden, jnp.zeros_like(hidden))
    hpad = jnp.pad(hidden, ((0, 0), (0, 0), (0, 0), (0, 1), (0, 0)))
    hflat = hpad.reshape(clips * frames, rows + 1, width + 1, channels)

    kernel2 = down_weight.reshape(3, 3, channels, channels)
    latent = lax.conv_general_dilated(
        hflat,
        kernel2,
        window_strides=(2, 2),
        padding="VALID",
        dimension_numbers=("NHWC", "HWIO", "NHWC"),
        preferred_element_type=jnp.float32,
    ).astype(jnp.bfloat16)
    latent = latent.reshape(cotangent.shape)

    cflat = cotangent.reshape(clips * frames, rows // 2, width // 2, channels)
    grad_down = lax.conv_general_dilated(
        hflat,
        cflat,
        window_strides=(1, 1),
        padding="VALID",
        rhs_dilation=(2, 2),
        dimension_numbers=("CHWN", "IHWO", "NHWC"),
        preferred_element_type=jnp.float32,
    )
    grad_down = jnp.transpose(grad_down, (1, 2, 0, 3)).reshape(9 * channels, channels)

    cot2 = jnp.concatenate([cot_above, cotangent], axis=2).reshape(
        clips * frames, rows // 2 + 1, width // 2, channels
    )
    d_hidden = lax.conv_general_dilated(
        cot2,
        kernel2[::-1, ::-1],
        window_strides=(1, 1),
        padding=((0, 1), (2, 1)),
        lhs_dilation=(2, 2),
        dimension_numbers=("NHWC", "HWOI", "NHWC"),
        preferred_element_type=jnp.float32,
    ).reshape(clips, frames, rows, width, channels)

    d_conv = norm_back(conv_out[:, :, :rows], norm_gain, keeper, d_hidden)
    grad_conv = lax.conv_general_dilated(
        padded[:, :, : rows + 2],
        d_conv,
        window_strides=(1, 1, 1),
        padding="VALID",
        dimension_numbers=("CDHWN", "IDHWO", "NDHWC"),
        preferred_element_type=jnp.float32,
    )
    grad_conv = jnp.transpose(grad_conv, (1, 2, 3, 0, 4)).reshape(27 * channels, channels)

    grad_conv, grad_down = lax.psum(
        (grad_conv.astype(jnp.bfloat16), grad_down.astype(jnp.bfloat16)), ("tm", "space")
    )
    devices = lax.axis_size("tm") * lax.axis_size("space")
    me = t * lax.axis_size("space") + s
    conv_rows = grad_conv.shape[0] // devices
    down_rows = grad_down.shape[0] // devices
    conv_share = lax.dynamic_slice_in_dim(grad_conv, me * conv_rows, conv_rows, axis=0)
    down_share = lax.dynamic_slice_in_dim(grad_down, me * down_rows, down_rows, axis=0)
    return (
        latent,
        conv_share.astype(jnp.float32).reshape(-1),
        down_share.astype(jnp.float32).reshape(-1),
    )


def solution(mesh):
    in_specs = (
        P(None, "tm", "space", None, None),
        P(),
        P(),
        P(),
        P(),
        P(None, "tm", "space", None, None),
    )
    out_specs = (P(None, "tm", "space", None, None), P(("tm", "space")), P(("tm", "space")))
    return jax.shard_map(local, mesh=mesh, in_specs=in_specs, out_specs=out_specs, check_vma=False)
```

```python
import jax
import jax.numpy as jnp
from jax import lax
from jax.sharding import PartitionSpec as P

EPSILON = 1e-06


def shifted(array, axes, moves):
    sizes = [lax.axis_size(a) for a in axes]
    total = 1
    for n in sizes:
        total *= n
    pairs = []
    for src in range(total):
        coords, rest = [], src
        for n in reversed(sizes):
            coords.append(rest % n)
            rest //= n
        coords = coords[::-1]
        dst = [c + m for c, m in zip(coords, moves)]
        if all(0 <= d < n for d, n in zip(dst, sizes)):
            flat = 0
            for d, n in zip(dst, sizes):
                flat = flat * n + d
            pairs.append((src, flat))
    name = axes[0] if len(axes) == 1 else tuple(axes)
    return lax.ppermute(array, name, pairs)


def norm_act(conv_out, norm_gain, keeper):
    scale = lax.rsqrt(jnp.mean(conv_out * conv_out, axis=-1, keepdims=True) + EPSILON)
    normed = conv_out * scale * norm_gain.astype(jnp.float32)
    return (normed * jax.nn.sigmoid(normed) * keeper).astype(jnp.bfloat16)


def norm_back(conv_out, norm_gain, keeper, upstream):
    scale = lax.rsqrt(jnp.mean(conv_out * conv_out, axis=-1, keepdims=True) + EPSILON)
    unit = conv_out * scale
    gained = norm_gain.astype(jnp.float32)
    normed = unit * gained
    sigma = jax.nn.sigmoid(normed)
    d_normed = upstream * keeper * sigma * (1.0 + normed * (1.0 - sigma))
    d_unit = d_normed * gained
    return (scale * (d_unit - unit * jnp.mean(d_unit * unit, axis=-1, keepdims=True))).astype(
        jnp.bfloat16
    )


def local(video, conv_weight, norm_gain, down_weight, clip_lengths, cotangent):
    clips, frames, rows, width, channels = video.shape
    t = lax.axis_index("tm")
    s = lax.axis_index("space")
    last = lax.axis_size("space") - 1
    frame_ids = t * frames + jnp.arange(frames, dtype=jnp.int32)
    keeper = (frame_ids[None, :] < clip_lengths[:, None]).astype(jnp.float32)[
        :, :, None, None, None
    ]
    masked = video * keeper.astype(jnp.bfloat16)

    top = masked[:, :, rows - 1 :]
    sent = jnp.concatenate([top, cotangent], axis=3)
    got = shifted(sent.reshape(-1, channels), ("space",), (1,)).reshape(sent.shape)
    above = got[:, :, :, :width]
    cot_above = got[:, :, :, width:]
    flat = masked.reshape(-1, channels)
    below = shifted(flat, ("space",), (-1,)).reshape(masked.shape)
    prev = shifted(flat, ("tm",), (1,)).reshape(masked.shape)
    prev_above = shifted(top.reshape(-1, channels), ("tm", "space"), (1, 1)).reshape(top.shape)
    prev_below = shifted(flat, ("tm", "space"), (1, -1)).reshape(masked.shape)

    own = jnp.concatenate([above, masked, below], axis=2)
    old = jnp.concatenate([prev_above, prev, prev_below], axis=2)
    padded = jnp.pad(
        jnp.concatenate([old, own], axis=1), ((0, 0), (0, 0), (0, 0), (1, 1), (0, 0))
    )

    kernel3 = conv_weight.reshape(3, 3, 3, channels, channels)
    conv_out = lax.conv_general_dilated(
        padded,
        kernel3,
        window_strides=(1, 1, 1),
        padding="VALID",
        dimension_numbers=("NDHWC", "DHWIO", "NDHWC"),
        preferred_element_type=jnp.float32,
    )
    hidden = norm_act(conv_out, norm_gain, keeper)
    row_ids = jnp.arange(rows + 1, dtype=jnp.int32)[None, None, :, None, None]
    hidden = jnp.where((row_ids < rows) | (s < last), hidden, jnp.zeros_like(hidden))
    hpad = jnp.pad(hidden, ((0, 0), (0, 0), (0, 0), (0, 1), (0, 0)))
    hflat = hpad.reshape(clips * frames, rows + 1, width + 1, channels)

    kernel2 = down_weight.reshape(3, 3, channels, channels)
    latent = lax.conv_general_dilated(
        hflat,
        kernel2,
        window_strides=(2, 2),
        padding="VALID",
        dimension_numbers=("NHWC", "HWIO", "NHWC"),
        preferred_element_type=jnp.float32,
    ).astype(jnp.bfloat16)
    latent = latent.reshape(cotangent.shape)

    cflat = cotangent.reshape(clips * frames, rows // 2, width // 2, channels)
    grad_down = lax.conv_general_dilated(
        hflat,
        cflat,
        window_strides=(1, 1),
        padding="VALID",
        rhs_dilation=(2, 2),
        dimension_numbers=("CHWN", "IHWO", "NHWC"),
        preferred_element_type=jnp.float32,
    )
    grad_down = jnp.transpose(grad_down, (1, 2, 0, 3)).reshape(9 * channels, channels)

    cot2 = jnp.concatenate([cot_above, cotangent], axis=2).reshape(
        clips * frames, rows // 2 + 1, width // 2, channels
    )
    d_hidden = lax.conv_general_dilated(
        cot2,
        kernel2[::-1, ::-1],
        window_strides=(1, 1),
        padding=((0, 1), (2, 1)),
        lhs_dilation=(2, 2),
        dimension_numbers=("NHWC", "HWOI", "NHWC"),
        preferred_element_type=jnp.float32,
    ).reshape(clips, frames, rows, width, channels)

    d_conv = norm_back(conv_out[:, :, :rows], norm_gain, keeper, d_hidden)
    grad_conv = lax.conv_general_dilated(
        padded[:, :, : rows + 2],
        d_conv,
        window_strides=(1, 1, 1),
        padding="VALID",
        dimension_numbers=("CDHWN", "IDHWO", "NDHWC"),
        preferred_element_type=jnp.float32,
    )
    grad_conv = jnp.transpose(grad_conv, (1, 2, 3, 0, 4)).reshape(27 * channels, channels)

    grad_conv, grad_down = lax.psum((grad_conv, grad_down), ("tm", "space"))
    devices = lax.axis_size("tm") * lax.axis_size("space")
    me = t * lax.axis_size("space") + s
    conv_rows = grad_conv.shape[0] // devices
    down_rows = grad_down.shape[0] // devices
    conv_share = lax.dynamic_slice_in_dim(grad_conv, me * conv_rows, conv_rows, axis=0)
    down_share = lax.dynamic_slice_in_dim(grad_down, me * down_rows, down_rows, axis=0)
    return (latent, conv_share.reshape(-1), down_share.reshape(-1))


def solution(mesh):
    in_specs = (
        P(None, "tm", "space", None, None),
        P(),
        P(),
        P(),
        P(),
        P(None, "tm", "space", None, None),
    )
    out_specs = (P(None, "tm", "space", None, None), P(("tm", "space")), P(("tm", "space")))
    return jax.shard_map(local, mesh=mesh, in_specs=in_specs, out_specs=out_specs, check_vma=False)
```

```python
import jax
import jax.numpy as jnp
from jax import lax
from jax.sharding import PartitionSpec as P

EPSILON = 1e-06


def shifted(array, axes, moves):
    sizes = [lax.axis_size(a) for a in axes]
    total = 1
    for n in sizes:
        total *= n
    pairs = []
    for src in range(total):
        coords, rest = [], src
        for n in reversed(sizes):
            coords.append(rest % n)
            rest //= n
        coords = coords[::-1]
        dst = [c + m for c, m in zip(coords, moves)]
        if all(0 <= d < n for d, n in zip(dst, sizes)):
            flat = 0
            for d, n in zip(dst, sizes):
                flat = flat * n + d
            pairs.append((src, flat))
    name = axes[0] if len(axes) == 1 else tuple(axes)
    return lax.ppermute(array, name, pairs)


def norm_act(conv_out, norm_gain, keeper):
    scale = lax.rsqrt(jnp.mean(conv_out * conv_out, axis=-1, keepdims=True) + EPSILON)
    normed = conv_out * scale * norm_gain.astype(jnp.float32)
    return (normed * jax.nn.sigmoid(normed) * keeper).astype(jnp.bfloat16)


def norm_back(conv_out, norm_gain, keeper, upstream):
    scale = lax.rsqrt(jnp.mean(conv_out * conv_out, axis=-1, keepdims=True) + EPSILON)
    unit = conv_out * scale
    gained = norm_gain.astype(jnp.float32)
    normed = unit * gained
    sigma = jax.nn.sigmoid(normed)
    d_normed = upstream * keeper * sigma * (1.0 + normed * (1.0 - sigma))
    d_unit = d_normed * gained
    return (scale * (d_unit - unit * jnp.mean(d_unit * unit, axis=-1, keepdims=True))).astype(
        jnp.bfloat16
    )


def local(video, conv_weight, norm_gain, down_weight, clip_lengths, cotangent):
    clips, frames, rows, width, channels = video.shape
    t = lax.axis_index("tm")
    s = lax.axis_index("space")
    last = lax.axis_size("space") - 1
    frame_ids = t * frames + jnp.arange(frames, dtype=jnp.int32)
    keeper = (frame_ids[None, :] < clip_lengths[:, None]).astype(jnp.float32)[
        :, :, None, None, None
    ]
    masked = video * keeper.astype(jnp.bfloat16)

    top = masked[:, :, rows - 1 :]
    sent = jnp.concatenate([top, cotangent], axis=3)
    got = shifted(sent.reshape(-1, channels), ("space",), (1,)).reshape(sent.shape)
    above = got[:, :, :, :width]
    cot_above = got[:, :, :, width:]
    flat = masked.reshape(-1, channels)
    below = shifted(flat, ("space",), (-1,)).reshape(masked.shape)
    prev = shifted(flat, ("tm",), (1,)).reshape(masked.shape)
    prev_above = shifted(top.reshape(-1, channels), ("tm", "space"), (1, 1)).reshape(top.shape)
    prev_below = shifted(flat, ("tm", "space"), (1, -1)).reshape(masked.shape)

    own = jnp.concatenate([above, masked, below], axis=2)
    old = jnp.concatenate([prev_above, prev, prev_below], axis=2)
    padded = jnp.pad(
        jnp.concatenate([old, own], axis=1), ((0, 0), (0, 0), (0, 0), (1, 1), (0, 0))
    )

    kernel3 = conv_weight.reshape(3, 3, 3, channels, channels)
    conv_out = lax.conv_general_dilated(
        padded,
        kernel3,
        window_strides=(1, 1, 1),
        padding="VALID",
        dimension_numbers=("NDHWC", "DHWIO", "NDHWC"),
        preferred_element_type=jnp.float32,
    )
    hidden = norm_act(conv_out, norm_gain, keeper)
    row_ids = jnp.arange(rows + 1, dtype=jnp.int32)[None, None, :, None, None]
    hidden = jnp.where((row_ids < rows) | (s < last), hidden, jnp.zeros_like(hidden))
    hpad = jnp.pad(hidden, ((0, 0), (0, 0), (0, 0), (0, 1), (0, 0)))
    hflat = hpad.reshape(clips * frames, rows + 1, width + 1, channels)

    kernel2 = down_weight.reshape(3, 3, channels, channels)
    latent = lax.conv_general_dilated(
        hflat,
        kernel2,
        window_strides=(2, 2),
        padding="VALID",
        dimension_numbers=("NHWC", "HWIO", "NHWC"),
        preferred_element_type=jnp.float32,
    ).astype(jnp.bfloat16)
    latent = latent.reshape(cotangent.shape)

    cflat = cotangent.reshape(clips * frames, rows // 2, width // 2, channels)
    grad_down = lax.conv_general_dilated(
        hflat,
        cflat,
        window_strides=(1, 1),
        padding="VALID",
        rhs_dilation=(2, 2),
        dimension_numbers=("CHWN", "IHWO", "NHWC"),
        preferred_element_type=jnp.float32,
    )
    grad_down = jnp.transpose(grad_down, (1, 2, 0, 3)).reshape(9 * channels, channels)
    grad_down = lax.psum(grad_down, ("tm", "space"))

    cot2 = jnp.concatenate([cot_above, cotangent], axis=2).reshape(
        clips * frames, rows // 2 + 1, width // 2, channels
    )
    d_hidden = lax.conv_general_dilated(
        cot2,
        kernel2[::-1, ::-1],
        window_strides=(1, 1),
        padding=((0, 1), (2, 1)),
        lhs_dilation=(2, 2),
        dimension_numbers=("NHWC", "HWOI", "NHWC"),
        preferred_element_type=jnp.float32,
    ).reshape(clips, frames, rows, width, channels)

    d_conv = norm_back(conv_out[:, :, :rows], norm_gain, keeper, d_hidden)
    grad_conv = lax.conv_general_dilated(
        padded[:, :, : rows + 2],
        d_conv,
        window_strides=(1, 1, 1),
        padding="VALID",
        dimension_numbers=("CDHWN", "IDHWO", "NDHWC"),
        preferred_element_type=jnp.float32,
    )
    grad_conv = jnp.transpose(grad_conv, (1, 2, 3, 0, 4)).reshape(27 * channels, channels)

    grad_down, grad_conv = lax.optimization_barrier((grad_down, grad_conv))
    grad_conv = lax.psum(grad_conv, ("tm", "space"))
    devices = lax.axis_size("tm") * lax.axis_size("space")
    me = t * lax.axis_size("space") + s
    conv_rows = grad_conv.shape[0] // devices
    down_rows = grad_down.shape[0] // devices
    conv_share = lax.dynamic_slice_in_dim(grad_conv, me * conv_rows, conv_rows, axis=0)
    down_share = lax.dynamic_slice_in_dim(grad_down, me * down_rows, down_rows, axis=0)
    return (latent, conv_share.reshape(-1), down_share.reshape(-1))


def solution(mesh):
    in_specs = (
        P(None, "tm", "space", None, None),
        P(),
        P(),
        P(),
        P(),
        P(None, "tm", "space", None, None),
    )
    out_specs = (P(None, "tm", "space", None, None), P(("tm", "space")), P(("tm", "space")))
    return jax.shard_map(local, mesh=mesh, in_specs=in_specs, out_specs=out_specs, check_vma=False)
```

```python
import jax
import jax.numpy as jnp
from jax import lax
from jax.sharding import PartitionSpec as P

EPSILON = 1e-06


def shifted(array, axes, moves):
    sizes = [lax.axis_size(a) for a in axes]
    total = 1
    for n in sizes:
        total *= n
    pairs = []
    for src in range(total):
        coords, rest = [], src
        for n in reversed(sizes):
            coords.append(rest % n)
            rest //= n
        coords = coords[::-1]
        dst = [c + m for c, m in zip(coords, moves)]
        if all(0 <= d < n for d, n in zip(dst, sizes)):
            flat = 0
            for d, n in zip(dst, sizes):
                flat = flat * n + d
            pairs.append((src, flat))
    name = axes[0] if len(axes) == 1 else tuple(axes)
    return lax.ppermute(array, name, pairs)


def norm_act(conv_out, norm_gain, keeper):
    scale = lax.rsqrt(jnp.mean(conv_out * conv_out, axis=-1, keepdims=True) + EPSILON)
    normed = conv_out * scale * norm_gain.astype(jnp.float32)
    return (normed * jax.nn.sigmoid(normed) * keeper).astype(jnp.bfloat16)


def norm_back(conv_out, norm_gain, keeper, upstream):
    scale = lax.rsqrt(jnp.mean(conv_out * conv_out, axis=-1, keepdims=True) + EPSILON)
    unit = conv_out * scale
    gained = norm_gain.astype(jnp.float32)
    normed = unit * gained
    sigma = jax.nn.sigmoid(normed)
    d_normed = upstream * keeper * sigma * (1.0 + normed * (1.0 - sigma))
    d_unit = d_normed * gained
    return (scale * (d_unit - unit * jnp.mean(d_unit * unit, axis=-1, keepdims=True))).astype(
        jnp.bfloat16
    )


def local(video, conv_weight, norm_gain, down_weight, clip_lengths, cotangent):
    clips, frames, rows, width, channels = video.shape
    t = lax.axis_index("tm")
    s = lax.axis_index("space")
    last = lax.axis_size("space") - 1
    frame_ids = t * frames + jnp.arange(frames, dtype=jnp.int32)
    keeper = (frame_ids[None, :] < clip_lengths[:, None]).astype(jnp.float32)[
        :, :, None, None, None
    ]
    prev_ids = frame_ids - frames
    prev_keeper = (prev_ids[None, :] < clip_lengths[:, None]).astype(jnp.bfloat16)[
        :, :, None, None, None
    ]

    top = video[:, :, rows - 1 :]
    sent = jnp.concatenate([top, cotangent], axis=3)
    got = shifted(sent.reshape(-1, channels), ("space",), (1,)).reshape(sent.shape)
    above = got[:, :, :, :width]
    cot_above = got[:, :, :, width:]
    flat = video.reshape(-1, channels)
    below = shifted(flat, ("space",), (-1,)).reshape(video.shape)
    prev = shifted(flat, ("tm",), (1,)).reshape(video.shape)
    prev_above = shifted(top.reshape(-1, channels), ("tm", "space"), (1, 1)).reshape(top.shape)
    prev_below = shifted(flat, ("tm", "space"), (1, -1)).reshape(video.shape)

    own = jnp.concatenate([above, video, below], axis=2) * keeper.astype(jnp.bfloat16)
    old = jnp.concatenate([prev_above, prev, prev_below], axis=2) * prev_keeper
    padded = jnp.pad(
        jnp.concatenate([old, own], axis=1), ((0, 0), (0, 0), (0, 0), (1, 1), (0, 0))
    )

    kernel3 = conv_weight.reshape(3, 3, 3, channels, channels)
    conv_out = lax.conv_general_dilated(
        padded,
        kernel3,
        window_strides=(1, 1, 1),
        padding="VALID",
        dimension_numbers=("NDHWC", "DHWIO", "NDHWC"),
        preferred_element_type=jnp.float32,
    )
    hidden = norm_act(conv_out, norm_gain, keeper)
    row_ids = jnp.arange(rows + 1, dtype=jnp.int32)[None, None, :, None, None]
    hidden = jnp.where((row_ids < rows) | (s < last), hidden, jnp.zeros_like(hidden))
    hpad = jnp.pad(hidden, ((0, 0), (0, 0), (0, 0), (0, 1), (0, 0)))
    hflat = hpad.reshape(clips * frames, rows + 1, width + 1, channels)

    kernel2 = down_weight.reshape(3, 3, channels, channels)
    latent = lax.conv_general_dilated(
        hflat,
        kernel2,
        window_strides=(2, 2),
        padding="VALID",
        dimension_numbers=("NHWC", "HWIO", "NHWC"),
        preferred_element_type=jnp.float32,
    ).astype(jnp.bfloat16)
    latent = latent.reshape(cotangent.shape)

    cflat = cotangent.reshape(clips * frames, rows // 2, width // 2, channels)
    grad_down = lax.conv_general_dilated(
        hflat,
        cflat,
        window_strides=(1, 1),
        padding="VALID",
        rhs_dilation=(2, 2),
        dimension_numbers=("CHWN", "IHWO", "NHWC"),
        preferred_element_type=jnp.float32,
    )
    grad_down = jnp.transpose(grad_down, (1, 2, 0, 3)).reshape(9 * channels, channels)

    cot2 = jnp.concatenate([cot_above, cotangent], axis=2).reshape(
        clips * frames, rows // 2 + 1, width // 2, channels
    )
    d_hidden = lax.conv_general_dilated(
        cot2,
        kernel2[::-1, ::-1],
        window_strides=(1, 1),
        padding=((0, 1), (2, 1)),
        lhs_dilation=(2, 2),
        dimension_numbers=("NHWC", "HWOI", "NHWC"),
        preferred_element_type=jnp.float32,
    ).reshape(clips, frames, rows, width, channels)

    d_conv = norm_back(conv_out[:, :, :rows], norm_gain, keeper, d_hidden)
    grad_conv = lax.conv_general_dilated(
        padded[:, :, : rows + 2],
        d_conv,
        window_strides=(1, 1, 1),
        padding="VALID",
        dimension_numbers=("CDHWN", "IDHWO", "NDHWC"),
        preferred_element_type=jnp.float32,
    )
    grad_conv = jnp.transpose(grad_conv, (1, 2, 3, 0, 4)).reshape(27 * channels, channels)

    grad_conv, grad_down = lax.psum((grad_conv, grad_down), ("tm", "space"))
    devices = lax.axis_size("tm") * lax.axis_size("space")
    me = t * lax.axis_size("space") + s
    conv_rows = grad_conv.shape[0] // devices
    down_rows = grad_down.shape[0] // devices
    conv_share = lax.dynamic_slice_in_dim(grad_conv, me * conv_rows, conv_rows, axis=0)
    down_share = lax.dynamic_slice_in_dim(grad_down, me * down_rows, down_rows, axis=0)
    return (latent, conv_share.reshape(-1), down_share.reshape(-1))


def solution(mesh):
    in_specs = (
        P(None, "tm", "space", None, None),
        P(),
        P(),
        P(),
        P(),
        P(None, "tm", "space", None, None),
    )
    out_specs = (P(None, "tm", "space", None, None), P(("tm", "space")), P(("tm", "space")))
    return jax.shard_map(local, mesh=mesh, in_specs=in_specs, out_specs=out_specs, check_vma=False)
```

```python
import jax
import jax.numpy as jnp
from jax import lax
from jax.sharding import PartitionSpec as P

EPSILON = 1e-06


def shifted(array, axes, moves):
    sizes = [lax.axis_size(a) for a in axes]
    total = 1
    for n in sizes:
        total *= n
    pairs = []
    for src in range(total):
        coords, rest = [], src
        for n in reversed(sizes):
            coords.append(rest % n)
            rest //= n
        coords = coords[::-1]
        dst = [c + m for c, m in zip(coords, moves)]
        if all(0 <= d < n for d, n in zip(dst, sizes)):
            flat = 0
            for d, n in zip(dst, sizes):
                flat = flat * n + d
            pairs.append((src, flat))
    name = axes[0] if len(axes) == 1 else tuple(axes)
    return lax.ppermute(array, name, pairs)


def norm_act(conv_out, norm_gain, keeper):
    scale = lax.rsqrt(jnp.mean(conv_out * conv_out, axis=-1, keepdims=True) + EPSILON)
    normed = conv_out * scale * norm_gain.astype(jnp.float32)
    return (normed * jax.nn.sigmoid(normed) * keeper).astype(jnp.bfloat16)


def norm_back(conv_out, norm_gain, keeper, upstream):
    scale = lax.rsqrt(jnp.mean(conv_out * conv_out, axis=-1, keepdims=True) + EPSILON)
    unit = conv_out * scale
    gained = norm_gain.astype(jnp.float32)
    normed = unit * gained
    sigma = jax.nn.sigmoid(normed)
    d_normed = upstream * keeper * sigma * (1.0 + normed * (1.0 - sigma))
    d_unit = d_normed * gained
    return (scale * (d_unit - unit * jnp.mean(d_unit * unit, axis=-1, keepdims=True))).astype(
        jnp.bfloat16
    )


def local(video, conv_weight, norm_gain, down_weight, clip_lengths, cotangent):
    clips, frames, rows, width, channels = video.shape
    t = lax.axis_index("tm")
    s = lax.axis_index("space")
    last = lax.axis_size("space") - 1
    frame_ids = t * frames + jnp.arange(frames, dtype=jnp.int32)
    keeper = (frame_ids[None, :] < clip_lengths[:, None]).astype(jnp.float32)[
        :, :, None, None, None
    ]
    masked = video * keeper.astype(jnp.bfloat16)

    top = masked[:, :, rows - 1 :]
    sent = jnp.concatenate([top, cotangent], axis=3)
    got = shifted(sent.reshape(-1, channels), ("space",), (1,)).reshape(sent.shape)
    above = got[:, :, :, :width]
    cot_above = got[:, :, :, width:]
    flat = masked.reshape(-1, channels)
    below = shifted(flat, ("space",), (-1,)).reshape(masked.shape)
    prev = shifted(flat, ("tm",), (1,)).reshape(masked.shape)
    prev_above = shifted(top.reshape(-1, channels), ("tm", "space"), (1, 1)).reshape(top.shape)
    prev_below = shifted(flat, ("tm", "space"), (1, -1)).reshape(masked.shape)

    own = jnp.concatenate([above, masked, below], axis=2)
    old = jnp.concatenate([prev_above, prev, prev_below], axis=2)
    padded = jnp.pad(
        jnp.concatenate([old, own], axis=1), ((0, 0), (0, 0), (0, 0), (1, 1), (0, 0))
    )

    kernel3 = conv_weight.reshape(3, 3, 3, channels, channels)
    conv_out = lax.conv_general_dilated(
        padded,
        kernel3,
        window_strides=(1, 1, 1),
        padding="VALID",
        dimension_numbers=("NDHWC", "DHWIO", "NDHWC"),
        preferred_element_type=jnp.float32,
    )
    hidden = norm_act(conv_out, norm_gain, keeper)
    row_ids = jnp.arange(rows + 1, dtype=jnp.int32)[None, None, :, None, None]
    hidden = jnp.where((row_ids < rows) | (s < last), hidden, jnp.zeros_like(hidden))
    hpad = jnp.pad(hidden, ((0, 0), (0, 0), (0, 0), (0, 1), (0, 0)))
    hflat = hpad.reshape(clips * frames, rows + 1, width + 1, channels)

    kernel2 = down_weight.reshape(3, 3, channels, channels)
    latent = lax.conv_general_dilated(
        hflat,
        kernel2,
        window_strides=(2, 2),
        padding="VALID",
        dimension_numbers=("NHWC", "HWIO", "NHWC"),
        preferred_element_type=jnp.float32,
    ).astype(jnp.bfloat16)
    latent = latent.reshape(cotangent.shape)

    cflat = cotangent.reshape(clips * frames, rows // 2, width // 2, channels)
    grad_down = lax.conv_general_dilated(
        hflat,
        cflat,
        window_strides=(1, 1),
        padding="VALID",
        rhs_dilation=(2, 2),
        dimension_numbers=("CHWN", "IHWO", "NHWC"),
        preferred_element_type=jnp.float32,
    )
    grad_down = jnp.transpose(grad_down, (1, 2, 0, 3)).reshape(9 * channels, channels)

    cot2 = jnp.concatenate([cot_above, cotangent], axis=2).reshape(
        clips * frames, rows // 2 + 1, width // 2, channels
    )
    d_hidden = lax.conv_general_dilated(
        cot2,
        kernel2[::-1, ::-1],
        window_strides=(1, 1),
        padding=((0, 1), (2, 1)),
        lhs_dilation=(2, 2),
        dimension_numbers=("NHWC", "HWOI", "NHWC"),
        preferred_element_type=jnp.float32,
    ).reshape(clips, frames, rows, width, channels)

    d_conv = norm_back(conv_out[:, :, :rows], norm_gain, keeper, d_hidden)
    grad_conv = lax.conv_general_dilated(
        padded[:, :, : rows + 2],
        d_conv,
        window_strides=(1, 1, 1),
        padding="VALID",
        dimension_numbers=("CDHWN", "IDHWO", "NDHWC"),
        preferred_element_type=jnp.float32,
    )
    grad_conv = jnp.transpose(grad_conv, (1, 2, 3, 0, 4)).reshape(27 * channels, channels)

    grad_conv, grad_down = lax.psum((grad_conv, grad_down), ("space", "tm"))
    devices = lax.axis_size("tm") * lax.axis_size("space")
    me = t * lax.axis_size("space") + s
    conv_rows = grad_conv.shape[0] // devices
    down_rows = grad_down.shape[0] // devices
    conv_share = lax.dynamic_slice_in_dim(grad_conv, me * conv_rows, conv_rows, axis=0)
    down_share = lax.dynamic_slice_in_dim(grad_down, me * down_rows, down_rows, axis=0)
    return (latent, conv_share.reshape(-1), down_share.reshape(-1))


def solution(mesh):
    in_specs = (
        P(None, "tm", "space", None, None),
        P(),
        P(),
        P(),
        P(),
        P(None, "tm", "space", None, None),
    )
    out_specs = (P(None, "tm", "space", None, None), P(("tm", "space")), P(("tm", "space")))
    return jax.shard_map(local, mesh=mesh, in_specs=in_specs, out_specs=out_specs, check_vma=False)
```
